256 devices in a mesh: dx: 8 (over y_hi, x), dy: 16 (over z, core), rep: 2 (over y_lo).
Axes of the slice: x: 4, y: 4 (y_hi: 2, y_lo: 2; y = y_hi * 2 + y_lo), z: 8, core: 2. Of those that a mesh axis runs over, the one named last changes fastest.
Arguments:
- species: int32 [2, 8, 16, 256], P('rep', 'dx', 'dy'), may hold values from 0 to 3
- positions: float32 [2, 8, 16, 3, 256], P('rep', 'dx', 'dy'), may hold values from 0 to 40, as said below
- send_idx: int32 [2, 8, 16, 128], P('rep', 'dx', 'dy'), may hold values from 0 to 255, as said below
- neighbours: int32 [2, 8, 16, 32, 256], P('rep', 'dx', 'dy'), may hold values from 0 to 1279, as said below
- neigh_count: int32 [2, 8, 16, 256], P('rep', 'dx', 'dy'), may hold values from 8 to 32, as said below
- energy_ref: float32 [2], P('rep'), may hold values from 2 to 4
- embed: bfloat16 [4, 128], replicated, may hold values from -6 to 6
- w_lin: bfloat16 [128, 128], replicated, may hold values from -0.5 to 0.5
- w_in: bfloat16 [8, 64], replicated, may hold values from -2 to 2
- w_mid: bfloat16 [64, 64], replicated, may hold values from -0.75 to 0.75
- w_out: bfloat16 [64, 384], replicated, may hold values from -0.75 to 0.75
- w_mix: bfloat16 [384, 128], replicated, may hold values from -0.3125 to 0.3125
- w_site: float32 [128], replicated, may hold values from -0.5 to 0.5
Outputs:
- forces: float32 [2, 8, 16, 3, 256], P('rep', 'dx', 'dy')
- energy: float32 [2], P('rep')
- grad_lin: float32 [128, 128], replicated
- grad_in: float32 [8, 64], replicated
- grad_mid: float32 [64, 64], replicated
- grad_out: float32 [64, 384], replicated
- grad_mix: float32 [384, 128], replicated
The draws below stay inside these ranges and needn't reach their ends.
Inputs may be any that keep to these rules, and one draw needn't show every extreme that they name: `positions`: x and y lie in [0, 7); z lies in [0, 40). send_idx[r,x,y,g] is 2 g or 2 g + 1. `neighbours`: slots below neigh_count name distinct seen atoms other than the atom itself; the last seen atom is named in every draw. `neigh_count`: in replica r every count lies between 8 and 32 - 8 r; replica 0 has an atom with all 32 slots live in every domain.
All inputs are finite; a program needn't handle non-finite values.
Results may differ from the reference program's by a relative error of at most 0.0003.
The reference program's roundings to bfloat16 on the way (of `lifted`, `basis` and `invariants`) count: a program that leaves them out, or rounds other values in their place, can miss the bound.
Values sent between devices are 32-bit elements; how exact they have to be, the bound alone decides.
No kernel may reach another device: no remote copies, remote signals or barrier semaphores. Data moves between devices by JAX's collectives and lax.ppermute only.
A program may use at most 128 MiB of HBM per device.

```python
import math
import jax
import jax.numpy as jnp
import numpy as np
from jax import lax

CHANNELS = 128
RBF = 8
RADIAL = 64
SPECIES = 4
NEIGH = 32
ATOMS = 256
GHOSTS = 128
REPS = 2
GRID_X = 8
GRID_Y = 16


def lattice_offsets():
    found = []
    for step_z in range(-2, 3):
        for step_y in range(-2, 3):
            for step_x in range(-2, 3):
                if step_x == 0 and step_y == 0 and (step_z == 0):
                    continue
                length = (1.75 * step_x) ** 2 + (1.75 * step_y) ** 2 + (2.5 * step_z) ** 2
                if length <= 25.0:
                    found.append((step_x, step_y, step_z))
    return np.array(found, dtype=np.int32)


def ghost_bits(key):
    return jax.random.randint(jax.random.fold_in(key, 11), (REPS, GRID_X, GRID_Y, GHOSTS), 0, 2)


def lattice_lists(key):
    table = lattice_offsets()
    width = table.shape[0]
    off_x = jnp.asarray(table[:, 0], dtype=jnp.int32)
    off_y = jnp.asarray(table[:, 1], dtype=jnp.int32)
    off_z = jnp.asarray(table[:, 2], dtype=jnp.int32)
    layers = ATOMS // 16
    atom = jnp.arange(ATOMS, dtype=jnp.int32)
    site_x = atom % 4
    site_y = atom // 4 % 4
    site_z = atom // 16
    reach_x = site_x[:, None] + off_x[None, :]
    reach_y = site_y[:, None] + off_y[None, :]
    reach_z = site_z[:, None] + off_z[None, :]
    side_x = jnp.floor_divide(reach_x, 4)
    side_y = jnp.floor_divide(reach_y, 4)
    target_x = reach_x - 4 * side_x
    target_y = reach_y - 4 * side_y
    inside_z = (reach_z >= 0) & (reach_z < layers)
    target_z = jnp.clip(reach_z, 0, layers - 1)
    target = target_z * 16 + target_y * 4 + target_x
    own = (side_x == 0) & (side_y == 0)
    slot = (side_x + 1) * 3 + (side_y + 1)
    slot = jnp.where(slot > 4, slot - 1, slot)
    slot = jnp.where(own, 0, slot)
    bits = ghost_bits(key)
    rolled = []
    for step_x in (-1, 0, 1):
        for step_y in (-1, 0, 1):
            if step_x == 0 and step_y == 0:
                continue
            rolled.append(jnp.roll(bits, (-step_x, -step_y), (1, 2)))
    rolled_all = jnp.stack(rolled, axis=3).reshape(REPS, GRID_X, GRID_Y, 8 * GHOSTS)
    lookup = (slot * GHOSTS + target // 2).reshape(-1)
    fetched = jnp.take(rolled_all, lookup, axis=3).reshape(REPS, GRID_X, GRID_Y, ATOMS, width)
    ghost_ok = fetched == (target % 2)[None, None, None]
    valid = inside_z[None, None, None] & (own[None, None, None] | ghost_ok)
    index = jnp.where(own, target, ATOMS + slot * GHOSTS + target // 2)
    index = jnp.broadcast_to(index[None, None, None], valid.shape)
    noise = jax.random.randint(jax.random.fold_in(key, 12), valid.shape, 0, 1 << 20)
    column = lax.broadcasted_iota(jnp.int32, valid.shape, 4)
    scores = jnp.where(valid, noise * 128 + column, -1)
    top_scores, picks = lax.top_k(scores, NEIGH)
    chosen = jnp.take_along_axis(index, picks, axis=4)
    avail = jnp.sum(valid.astype(jnp.int32), axis=4)
    slot_ids = lax.broadcasted_iota(jnp.int32, chosen.shape, 4)
    self_ids = jnp.broadcast_to(atom[None, None, None, :, None], chosen.shape)
    chosen = jnp.where(slot_ids < avail[..., None], chosen, self_ids)
    shape_all = (REPS, GRID_X, GRID_Y, ATOMS)
    replica_ids = lax.broadcasted_iota(jnp.int32, shape_all, 0)
    upper_end = NEIGH - replica_ids * (NEIGH // (2 * REPS)) + 1
    lower_end = NEIGH // 4
    random_bits = jax.random.randint(jax.random.fold_in(key, 13), shape_all, 0, 1 << 20)
    counts = jnp.minimum(lower_end + random_bits % (upper_end - lower_end), avail)
    special = layers // 2 * 16 + 5
    counts = counts.at[0, :, :, special].set(NEIGH)
    chosen = chosen.at[0, :, :, special, NEIGH - 1].set(ATOMS + 8 * GHOSTS - 1)
    return (jnp.swapaxes(chosen, 3, 4), counts)


def draw_send_idx(key, part):
    bits = ghost_bits(key)
    return 2 * lax.broadcasted_iota(jnp.int32, bits.shape, 3) + bits


def draw_neighbours(key, part):
    return lattice_lists(key)[0]


def draw_neigh_count(key, part):
    return lattice_lists(key)[1]


def draw_positions(key, part):
    shape_all = (REPS, GRID_X, GRID_Y, 3, ATOMS)
    atom = lax.broadcasted_iota(jnp.int32, shape_all, 4)
    axis_id = lax.broadcasted_iota(jnp.int32, shape_all, 3)
    cell = jnp.where(axis_id == 0, atom % 4, jnp.where(axis_id == 1, atom // 4 % 4, atom // 16)).astype(jnp.float32)
    spacing = jnp.where(axis_id == 2, 2.5, 1.75).astype(jnp.float32)
    raw = jax.random.uniform(jax.random.fold_in(key, 14), shape_all, jnp.float32, -1.0, 1.0)
    jitter = 0.3 * raw
    return ((cell + 0.5 + jitter) * spacing).astype(jnp.float32)


def touch_ends(drawn, rng, smallest, top_value):
    place = [jax.random.randint(jax.random.fold_in(rng, axis), (), 0, length) for axis, length in enumerate(drawn.shape)]
    main_axis = drawn.shape.index(max(drawn.shape))
    neighbour = place[:main_axis] + [(place[main_axis] + 1) % drawn.shape[main_axis]] + place[main_axis + 1:]
    return drawn.at[tuple(place)].set(smallest).at[tuple(neighbour)].set(top_value)


def steps_of(own_key, dims, split, smallest, high):
    factor_of = 1.0
    for axis_at, blocks in split:
        draws = jax.random.uniform(jax.random.fold_in(jax.random.fold_in(own_key, 6), axis_at), (blocks,), jnp.float32, smallest / len(split), high / len(split))
        factor_of = factor_of * jnp.repeat(jnp.exp(draws), dims[axis_at] // blocks).reshape((-1,) + (1,) * (len(dims) - 1 - axis_at))
    return factor_of


def centred(rng, shape, scale, reach, kind=jnp.bfloat16):
    return jnp.clip(scale * jax.random.normal(rng, shape, jnp.float32), -reach, reach).astype(kind)


def setup_inputs(seed: int = 0) -> dict:
    keys = jax.random.split(jax.random.key(seed), 14)
    species = touch_ends(jax.random.randint(keys[0], (REPS, GRID_X, GRID_Y, ATOMS), 0, SPECIES), jax.random.fold_in(keys[0], 1), 0, SPECIES - 1).astype(jnp.int32)
    positions = draw_positions(jax.random.fold_in(keys[13], 71), 0)
    send_idx = draw_send_idx(jax.random.fold_in(keys[13], 71), 0)
    neighbours = draw_neighbours(jax.random.fold_in(keys[13], 71), 0)
    neigh_count = draw_neigh_count(jax.random.fold_in(keys[13], 71), 0)
    energy_ref = jnp.clip(2.0 + 2.0 * jax.random.uniform(keys[5], (REPS,), jnp.float32) ** steps_of(keys[5], (REPS,), ((0, 2),), -0.2, 0.2), 2.0, 4.0)
    embed = centred(keys[6], (SPECIES, CHANNELS), 1.0, 6.0)
    w_lin = centred(keys[7], (CHANNELS, CHANNELS), CHANNELS ** -0.5, 0.5)
    w_in = centred(keys[8], (RBF, RADIAL), RBF ** -0.5, 2.0)
    w_mid = centred(keys[9], (RADIAL, RADIAL), RADIAL ** -0.5, 0.75)
    w_out = centred(keys[10], (RADIAL, 3 * CHANNELS), RADIAL ** -0.5, 0.75)
    w_mix = centred(keys[11], (3 * CHANNELS, CHANNELS), (3 * CHANNELS) ** -0.5, 0.3125)
    w_site = centred(keys[12], (CHANNELS,), CHANNELS ** -0.5, 0.5, jnp.float32)
    return dict(species=species, positions=positions, send_idx=send_idx, neighbours=neighbours, neigh_count=neigh_count, energy_ref=energy_ref, embed=embed, w_lin=w_lin, w_in=w_in, w_mid=w_mid, w_out=w_out, w_mix=w_mix, w_site=w_site)


HIGHEST = lax.Precision.HIGHEST
cutoff_top = 6.0
cutoff_sq = 36.0
width_gain = 2.0
domain_side = 7.0
root_three = math.sqrt(3.0)
root_five = math.sqrt(5.0)
root_fifteen = math.sqrt(15.0)

def rounded(values):
    narrow = lax.optimization_barrier(values.astype(jnp.bfloat16))
    return values + lax.stop_gradient(narrow.astype(jnp.float32) - values)

def apply_left(weight, values):
    return lax.dot_general(weight, values, (((0,), (0,)), ((), ())), precision=HIGHEST)

def block_energy(seen_feat, seen_pos, neigh_blk, count_blk, base_blk, own_pos, weights):
    w_in, w_mid, w_out, w_mix, w_site = weights
    slots, atoms_blk = neigh_blk.shape
    chans = base_blk.shape[0]
    flat_index = neigh_blk.reshape(-1)
    far_pos = jnp.take(seen_pos, flat_index, axis=1)
    near_pos = jnp.broadcast_to(own_pos[:, None, :], (3, slots, atoms_blk)).reshape(3, slots * atoms_blk)
    delta = far_pos - near_pos
    dist_sq = lax.optimization_barrier(jnp.sum(delta * delta, axis=0)) + 0.01
    radius = jnp.sqrt(dist_sq)
    unit = delta / radius[None, :]
    nbasis = w_in.shape[0]
    centres = cutoff_top * jnp.arange(nbasis, dtype=jnp.float32) / (nbasis - 1)
    envelope = jnp.maximum(1.0 - dist_sq / cutoff_sq, 0.0) ** 2
    basis = rounded(jnp.exp(-width_gain * (radius[None, :] - centres[:, None]) ** 2) * envelope[None, :])
    first = rounded(jax.nn.silu(apply_left(w_in, basis)))
    second = rounded(jax.nn.silu(apply_left(w_mid, first)))
    radial = apply_left(w_out, second)
    live = (lax.broadcasted_iota(jnp.int32, (slots, atoms_blk), 0) < count_blk[None, :]).astype(jnp.float32).reshape(-1)
    sender = jnp.take(seen_feat, flat_index, axis=1) * live[None, :]
    unit_x = unit[0]
    unit_y = unit[1]
    unit_z = unit[2]
    order_one = [root_three * unit_x, root_three * unit_y, root_three * unit_z]
    order_two = [root_fifteen * unit_x * unit_y, root_fifteen * unit_y * unit_z, 0.5 * root_five * (3.0 * unit_z * unit_z - 1.0), root_fifteen * unit_x * unit_z, 0.5 * root_fifteen * (unit_x * unit_x - unit_y * unit_y)]
    norm_gain = 1.0 / math.sqrt(slots)

    def pooled(values):
        return lax.optimization_barrier(jnp.sum(values.reshape(chans, slots, atoms_blk), axis=1)) * norm_gain
    scalar_part = pooled(radial[:chans] * sender)
    vector_msg = radial[chans:2 * chans] * sender
    tensor_msg = radial[2 * chans:] * sender
    vector_part = jnp.zeros_like(scalar_part)
    for harmonic in order_one:
        vector_part = vector_part + pooled(vector_msg * harmonic[None, :]) ** 2
    tensor_part = jnp.zeros_like(scalar_part)
    for harmonic in order_two:
        tensor_part = tensor_part + pooled(tensor_msg * harmonic[None, :]) ** 2
    invariants = rounded(jnp.concatenate([scalar_part, vector_part, tensor_part], axis=0))
    updated = base_blk + apply_left(w_mix, invariants)
    return jnp.sum(w_site[:, None] * jax.nn.silu(updated))

def local_energy(seen_feat, seen_pos, neigh, counts, base, weights):
    atoms = neigh.shape[1]
    block = min(atoms, 128)

    def one_block(index):
        start = index * block
        return block_energy(seen_feat, seen_pos, lax.dynamic_slice_in_dim(neigh, start, block, 1), lax.dynamic_slice_in_dim(counts, start, block, 0), lax.dynamic_slice_in_dim(base, start, block, 1), lax.dynamic_slice_in_dim(seen_pos, start, block, 1), weights)
    return jnp.sum(lax.map(jax.checkpoint(one_block), jnp.arange(atoms // block, dtype=jnp.int32)))

def replica_energy(coords, lin_w, in_w, mid_w, out_w, mix_w, kinds, send_list, neigh, counts, table, site_w):
    base = jnp.swapaxes(jnp.take(table, kinds, axis=0), 2, 3)
    lifted = rounded(jnp.einsum('io,xyia->xyoa', lin_w, base, precision=HIGHEST))
    pick = jax.vmap(jax.vmap(lambda values, chosen: jnp.take(values, chosen, axis=1)))
    sent_feat = pick(lifted, send_list)
    sent_pos = pick(coords, send_list)
    feat_parts = [lifted]
    pos_parts = [coords]
    for row in range(3):
        for column in range(3):
            if row == 1 and column == 1:
                continue
            step_x = row - 1
            step_y = column - 1
            feat_parts.append(jnp.roll(sent_feat, (-step_x, -step_y), (0, 1)))
            offset = jnp.asarray([domain_side * step_x, domain_side * step_y, 0.0], dtype=jnp.float32)
            pos_parts.append(jnp.roll(sent_pos, (-step_x, -step_y), (0, 1)) + offset[None, None, :, None])
    seen_feat = jnp.concatenate(feat_parts, axis=3)
    seen_pos = jnp.concatenate(pos_parts, axis=3)
    domains = kinds.shape[0] * kinds.shape[1]
    weights = (in_w, mid_w, out_w, mix_w, site_w)

    def per_domain(item):
        feat_one, pos_one, neigh_one, count_one, base_one = item
        return local_energy(feat_one, pos_one, neigh_one, count_one, base_one, weights)
    items = (seen_feat.reshape((domains,) + seen_feat.shape[2:]), seen_pos.reshape((domains,) + seen_pos.shape[2:]), neigh.reshape((domains,) + neigh.shape[2:]), counts.reshape((domains,) + counts.shape[2:]), base.reshape((domains,) + base.shape[2:]))
    return jnp.sum(lax.map(jax.checkpoint(per_domain), items))

def reference(species, positions, send_idx, neighbours, neigh_count, energy_ref, embed, w_lin, w_in, w_mid, w_out, w_mix, w_site):
    table = embed.astype(jnp.float32)
    site_w = w_site.astype(jnp.float32)
    reps = species.shape[0]
    trained = [weight.astype(jnp.float32) for weight in (w_lin, w_in, w_mid, w_out, w_mix)]
    stacked = [jnp.broadcast_to(weight[None], (reps,) + weight.shape) for weight in trained]

    def all_energy(coords, lin_s, in_s, mid_s, out_s, mix_s):
        mapped = jax.vmap(replica_energy, in_axes=(0, 0, 0, 0, 0, 0, 0, 0, 0, 0, None, None))
        return mapped(coords, lin_s, in_s, mid_s, out_s, mix_s, species, send_idx, neighbours, neigh_count, table, site_w)
    energies, pullback = jax.vjp(all_energy, positions, *stacked)
    cotangents = pullback(jnp.ones_like(energies))
    natoms = float(species.shape[1] * species.shape[2] * species.shape[3])
    per_atom = energies / natoms
    coef = (per_atom - energy_ref) / natoms
    grads = [lax.optimization_barrier(jnp.sum(coef.reshape((reps,) + (1,) * (grad_part.ndim - 1)) * grad_part, axis=0)) for grad_part in cotangents[1:]]
    return (-cotangents[0], per_atom, grads[0], grads[1], grads[2], grads[3], grads[4])
```

```python
import math

import jax
import jax.numpy as jnp
from jax import lax
from jax.sharding import PartitionSpec as P

HIGHEST = lax.Precision.HIGHEST
cutoff_top = 6.0
cutoff_sq = 36.0
width_gain = 2.0
domain_side = 7.0
root_three = math.sqrt(3.0)
root_five = math.sqrt(5.0)
root_fifteen = math.sqrt(15.0)
neighbour_steps = ((-1, -1), (-1, 0), (-1, 1), (0, -1), (0, 1), (1, -1), (1, 0), (1, 1))


def with_halo(shard, sides, width):
    for axis, dim in sides:
        count, length = (lax.axis_size(axis), shard.shape[dim])
        up = [(i, (i + 1) % count) for i in range(count)]
        down = [(j, i) for i, j in up]
        last = lax.slice_in_dim(shard, length - width, length, axis=dim)
        first = lax.slice_in_dim(shard, 0, width, axis=dim)
        before = lax.ppermute(last, axis, up)
        after = lax.ppermute(first, axis, down)
        shard = jnp.concatenate([before, shard, after], axis=dim)
    return shard


def rounded(values):
    narrow = lax.optimization_barrier(values.astype(jnp.bfloat16))
    return values + lax.stop_gradient(narrow.astype(jnp.float32) - values)


def apply_left(weight, values):
    return lax.dot_general(weight, values, (((0,), (0,)), ((), ())), precision=HIGHEST)


def block_energy(seen_feat, seen_pos, neigh_blk, count_blk, base_blk, own_pos, weights):
    w_in, w_mid, w_out, w_mix, w_site = weights
    slots, atoms_blk = neigh_blk.shape
    chans = base_blk.shape[0]
    flat_index = neigh_blk.reshape(-1)
    far_pos = jnp.take(seen_pos, flat_index, axis=1)
    near_pos = jnp.broadcast_to(own_pos[:, None, :], (3, slots, atoms_blk)).reshape(
        3, slots * atoms_blk
    )
    delta = far_pos - near_pos
    dist_sq = jnp.sum(delta * delta, axis=0) + 0.01
    radius = jnp.sqrt(dist_sq)
    unit = delta / radius[None, :]
    nbasis = w_in.shape[0]
    centres = cutoff_top * jnp.arange(nbasis, dtype=jnp.float32) / (nbasis - 1)
    envelope = jnp.maximum(1.0 - dist_sq / cutoff_sq, 0.0) ** 2
    basis = rounded(
        jnp.exp(-width_gain * (radius[None, :] - centres[:, None]) ** 2) * envelope[None, :]
    )
    first = rounded(jax.nn.silu(apply_left(w_in, basis)))
    second = rounded(jax.nn.silu(apply_left(w_mid, first)))
    radial = apply_left(w_out, second)
    live = (
        (lax.broadcasted_iota(jnp.int32, (slots, atoms_blk), 0) < count_blk[None, :])
        .astype(jnp.float32)
        .reshape(-1)
    )
    sender = jnp.take(seen_feat, flat_index, axis=1) * live[None, :]
    unit_x = unit[0]
    unit_y = unit[1]
    unit_z = unit[2]
    order_one = [root_three * unit_x, root_three * unit_y, root_three * unit_z]
    order_two = [
        root_fifteen * unit_x * unit_y,
        root_fifteen * unit_y * unit_z,
        0.5 * root_five * (3.0 * unit_z * unit_z - 1.0),
        root_fifteen * unit_x * unit_z,
        0.5 * root_fifteen * (unit_x * unit_x - unit_y * unit_y),
    ]
    norm_gain = 1.0 / math.sqrt(slots)

    def pooled(values):
        return jnp.sum(values.reshape(chans, slots, atoms_blk), axis=1) * norm_gain

    scalar_part = pooled(radial[:chans] * sender)
    vector_msg = radial[chans : 2 * chans] * sender
    tensor_msg = radial[2 * chans :] * sender
    vector_part = jnp.zeros_like(scalar_part)
    for harmonic in order_one:
        vector_part = vector_part + pooled(vector_msg * harmonic[None, :]) ** 2
    tensor_part = jnp.zeros_like(scalar_part)
    for harmonic in order_two:
        tensor_part = tensor_part + pooled(tensor_msg * harmonic[None, :]) ** 2
    invariants = rounded(jnp.concatenate([scalar_part, vector_part, tensor_part], axis=0))
    updated = base_blk + apply_left(w_mix, invariants)
    return jnp.sum(w_site[:, None] * jax.nn.silu(updated))


def local_energy(seen_feat, seen_pos, neigh, counts, base, weights):
    atoms = neigh.shape[1]
    block = min(atoms, 128)

    def one_block(index):
        start = index * block
        return block_energy(
            seen_feat,
            seen_pos,
            lax.dynamic_slice_in_dim(neigh, start, block, 1),
            lax.dynamic_slice_in_dim(counts, start, block, 0),
            lax.dynamic_slice_in_dim(base, start, block, 1),
            lax.dynamic_slice_in_dim(seen_pos, start, block, 1),
            weights,
        )

    return jnp.sum(lax.map(jax.checkpoint(one_block), jnp.arange(atoms // block, dtype=jnp.int32)))


def slot_list(beside_all):
    return [beside_all[step_x + 1, step_y + 1] for step_x, step_y in neighbour_steps]


def fold_slots(blocks, width):
    pieces = [blocks[:, slot * width : (slot + 1) * width] for slot in range(8)]
    empty = jnp.zeros_like(pieces[0])
    ordered = pieces[:4] + [empty] + pieces[4:]
    return jnp.stack(ordered, axis=0).reshape((3, 3) + pieces[0].shape)


def carry_features(slots):
    rows = with_halo(slots, (("dx", 0),), 1)
    merged = slots[1] + rows[0] + rows[4]
    columns = with_halo(merged, (("dy", 0),), 1)
    return merged[1] + columns[0] + columns[4]


def body(
    species,
    positions,
    send_idx,
    neighbours,
    neigh_count,
    energy_ref,
    embed,
    w_lin,
    w_in,
    w_mid,
    w_out,
    w_mix,
    w_site,
):
    kinds = species[0, 0, 0]
    coords = positions[0, 0, 0]
    send_list = send_idx[0, 0, 0]
    neigh = neighbours[0, 0, 0]
    counts = neigh_count[0, 0, 0]
    atoms = kinds.shape[0]
    ghosts = send_list.shape[0]
    table = embed.astype(jnp.float32)
    kind_grid = jnp.arange(table.shape[0], dtype=jnp.float32)
    own_hot = (kinds.astype(jnp.float32)[None, :] == kind_grid[:, None]).astype(jnp.float32)
    base = apply_left(table, own_hot)
    chans = base.shape[0]
    lin_w = w_lin.astype(jnp.float32)
    in_w = w_in.astype(jnp.float32)
    mid_w = w_mid.astype(jnp.float32)
    out_w = w_out.astype(jnp.float32)
    mix_w = w_mix.astype(jnp.float32)
    lifted = rounded(apply_left(lin_w, base))
    send_hot = (send_list[:, None] == lax.broadcasted_iota(jnp.int32, (ghosts, atoms), 1)).astype(
        jnp.float32
    )
    sent_pos = jnp.take(coords, send_list, axis=1)
    shift_rows = jnp.concatenate(
        [
            jnp.broadcast_to(
                jnp.asarray([domain_side * step_x, domain_side * step_y, 0.0], dtype=jnp.float32)[
                    :, None
                ],
                (3, ghosts),
            )
            for step_x, step_y in neighbour_steps
        ],
        axis=1,
    )

    def energy_of(own_feat, own_pos, far_feat, far_pos, p_in, p_mid, p_out, p_mix):
        seen_feat = jnp.concatenate([own_feat, far_feat], axis=1)
        seen_pos = jnp.concatenate([own_pos, far_pos], axis=1)
        return local_energy(
            seen_feat, seen_pos, neigh, counts, base, (p_in, p_mid, p_out, p_mix, w_site)
        )

    payload = jnp.concatenate([jnp.take(lifted, send_list, axis=1), sent_pos], axis=0)[None, None]
    beside_all = with_halo(payload, (("dx", 0), ("dy", 1)), 1)
    received = jnp.concatenate(slot_list(beside_all), axis=1)
    far_feat = received[:chans]
    far_pos = received[chans:] + shift_rows
    local_sum, pullback = jax.vjp(
        energy_of, lifted, coords, far_feat, far_pos, in_w, mid_w, out_w, mix_w
    )
    feat_own, pos_own, feat_far, pos_far, grad_in, grad_mid, grad_out, grad_mix = pullback(
        jnp.ones_like(local_sum)
    )
    slots = fold_slots(jnp.concatenate([feat_far, pos_far], axis=0), ghosts)
    returned = carry_features(slots)
    feat_total = feat_own + jnp.dot(returned[:chans], send_hot, precision=HIGHEST)
    pos_total = pos_own + jnp.dot(returned[chans:], send_hot, precision=HIGHEST)
    kind_sums = lax.dot_general(own_hot, feat_total, (((1,), (1,)), ((), ())), precision=HIGHEST)
    natoms = float(atoms * lax.axis_size("dx") * lax.axis_size("dy"))
    lane = 128
    first_site = (lax.axis_index("dx") == 0) & (lax.axis_index("dy") == 0)
    ref_part = jnp.where(first_site, energy_ref[0], 0.0)
    energy_row = jnp.zeros((1, lane), jnp.float32).at[0, 0].set(local_sum).at[0, 1].set(ref_part)
    parts = (kind_sums, grad_in, grad_mid, grad_out, grad_mix)
    packed = jnp.concatenate([g.reshape(-1, lane) for g in parts] + [energy_row], axis=0)
    reps = lax.axis_size("rep")
    rep_idx = lax.axis_index("rep")
    slot_hot = (jnp.arange(reps, dtype=jnp.int32) == rep_idx)[:, None, None]
    gathered = lax.psum(jnp.where(slot_hot, packed[None], 0.0), ("dx", "dy", "rep"))
    per_atom_all = gathered[:, -1, 0] / natoms
    coef_all = (per_atom_all - gathered[:, -1, 1]) / natoms
    weighted = jnp.sum(coef_all[:, None, None] * gathered[:, :-1], axis=0)
    outs = []
    offset = 0
    for g in parts:
        rows = g.size // lane
        outs.append(weighted[offset : offset + rows].reshape(g.shape))
        offset += rows
    grad_lin = lax.dot_general(table, outs[0], (((0,), (0,)), ((), ())), precision=HIGHEST)
    per_atom = jnp.sum(jnp.where(slot_hot[:, 0, 0], per_atom_all, 0.0))
    forces = (-pos_total)[None, None, None]
    return (forces, per_atom.reshape(1), grad_lin, outs[1], outs[2], outs[3], outs[4])


def solution(mesh):
    in_specs = (
        P("rep", "dx", "dy", None),
        P("rep", "dx", "dy", None, None),
        P("rep", "dx", "dy", None),
        P("rep", "dx", "dy", None, None),
        P("rep", "dx", "dy", None),
        P("rep"),
        P(),
        P(),
        P(),
        P(),
        P(),
        P(),
        P(),
    )
    out_specs = (P("rep", "dx", "dy", None, None), P("rep"), P(), P(), P(), P(), P())
    return jax.shard_map(body, mesh=mesh, in_specs=in_specs, out_specs=out_specs, check_vma=False)
```

```python
import math

import jax
import jax.numpy as jnp
from jax import lax
from jax.sharding import PartitionSpec as P

HIGHEST = lax.Precision.HIGHEST
cutoff_top = 6.0
cutoff_sq = 36.0
width_gain = 2.0
domain_side = 7.0
root_three = math.sqrt(3.0)
root_five = math.sqrt(5.0)
root_fifteen = math.sqrt(15.0)
neighbour_steps = ((-1, -1), (-1, 0), (-1, 1), (0, -1), (0, 1), (1, -1), (1, 0), (1, 1))


def with_halo(shard, sides, width):
    for axis, dim in sides:
        count, length = (lax.axis_size(axis), shard.shape[dim])
        up = [(i, (i + 1) % count) for i in range(count)]
        down = [(j, i) for i, j in up]
        last = lax.slice_in_dim(shard, length - width, length, axis=dim)
        first = lax.slice_in_dim(shard, 0, width, axis=dim)
        before = lax.ppermute(last, axis, up)
        after = lax.ppermute(first, axis, down)
        shard = jnp.concatenate([before, shard, after], axis=dim)
    return shard


def exchange_sum(values, axis):
    count = lax.axis_size(axis)
    assert count & (count - 1) == 0
    step = 1
    while step < count:
        values = values + lax.ppermute(values, axis, [(i, i ^ step) for i in range(count)])
        step *= 2
    return values


def rounded(values):
    narrow = lax.optimization_barrier(values.astype(jnp.bfloat16))
    return values + lax.stop_gradient(narrow.astype(jnp.float32) - values)


def apply_left(weight, values):
    return lax.dot_general(weight, values, (((0,), (0,)), ((), ())), precision=HIGHEST)


def block_energy(seen_feat, seen_pos, neigh_blk, count_blk, base_blk, own_pos, weights):
    w_in, w_mid, w_out, w_mix, w_site = weights
    slots, atoms_blk = neigh_blk.shape
    chans = base_blk.shape[0]
    flat_index = neigh_blk.reshape(-1)
    far_pos = jnp.take(seen_pos, flat_index, axis=1)
    near_pos = jnp.broadcast_to(own_pos[:, None, :], (3, slots, atoms_blk)).reshape(
        3, slots * atoms_blk
    )
    delta = far_pos - near_pos
    dist_sq = jnp.sum(delta * delta, axis=0) + 0.01
    radius = jnp.sqrt(dist_sq)
    unit = delta / radius[None, :]
    nbasis = w_in.shape[0]
    centres = cutoff_top * jnp.arange(nbasis, dtype=jnp.float32) / (nbasis - 1)
    envelope = jnp.maximum(1.0 - dist_sq / cutoff_sq, 0.0) ** 2
    basis = rounded(
        jnp.exp(-width_gain * (radius[None, :] - centres[:, None]) ** 2) * envelope[None, :]
    )
    first = rounded(jax.nn.silu(apply_left(w_in, basis)))
    second = rounded(jax.nn.silu(apply_left(w_mid, first)))
    radial = apply_left(w_out, second)
    live = (
        (lax.broadcasted_iota(jnp.int32, (slots, atoms_blk), 0) < count_blk[None, :])
        .astype(jnp.float32)
        .reshape(-1)
    )
    sender = jnp.take(seen_feat, flat_index, axis=1) * live[None, :]
    unit_x = unit[0]
    unit_y = unit[1]
    unit_z = unit[2]
    order_one = [root_three * unit_x, root_three * unit_y, root_three * unit_z]
    order_two = [
        root_fifteen * unit_x * unit_y,
        root_fifteen * unit_y * unit_z,
        0.5 * root_five * (3.0 * unit_z * unit_z - 1.0),
        root_fifteen * unit_x * unit_z,
        0.5 * root_fifteen * (unit_x * unit_x - unit_y * unit_y),
    ]
    norm_gain = 1.0 / math.sqrt(slots)

    def pooled(values):
        return jnp.sum(values.reshape(chans, slots, atoms_blk), axis=1) * norm_gain

    scalar_part = pooled(radial[:chans] * sender)
    vector_msg = radial[chans : 2 * chans] * sender
    tensor_msg = radial[2 * chans :] * sender
    vector_part = jnp.zeros_like(scalar_part)
    for harmonic in order_one:
        vector_part = vector_part + pooled(vector_msg * harmonic[None, :]) ** 2
    tensor_part = jnp.zeros_like(scalar_part)
    for harmonic in order_two:
        tensor_part = tensor_part + pooled(tensor_msg * harmonic[None, :]) ** 2
    invariants = rounded(jnp.concatenate([scalar_part, vector_part, tensor_part], axis=0))
    updated = base_blk + apply_left(w_mix, invariants)
    return jnp.sum(w_site[:, None] * jax.nn.silu(updated))


def local_energy(seen_feat, seen_pos, neigh, counts, base, weights):
    atoms = neigh.shape[1]
    block = min(atoms, 128)

    def one_block(index):
        start = index * block
        return block_energy(
            seen_feat,
            seen_pos,
            lax.dynamic_slice_in_dim(neigh, start, block, 1),
            lax.dynamic_slice_in_dim(counts, start, block, 0),
            lax.dynamic_slice_in_dim(base, start, block, 1),
            lax.dynamic_slice_in_dim(seen_pos, start, block, 1),
            weights,
        )

    return jnp.sum(lax.map(jax.checkpoint(one_block), jnp.arange(atoms // block, dtype=jnp.int32)))


def slot_list(beside_all):
    return [beside_all[step_x + 1, step_y + 1] for step_x, step_y in neighbour_steps]


def fold_slots(blocks, width):
    pieces = [blocks[:, slot * width : (slot + 1) * width] for slot in range(8)]
    empty = jnp.zeros_like(pieces[0])
    ordered = pieces[:4] + [empty] + pieces[4:]
    return jnp.stack(ordered, axis=0).reshape((3, 3) + pieces[0].shape)


def carry_features(slots):
    rows = with_halo(slots, (("dx", 0),), 1)
    merged = slots[1] + rows[0] + rows[4]
    columns = with_halo(merged, (("dy", 0),), 1)
    return merged[1] + columns[0] + columns[4]


def body(
    species,
    positions,
    send_idx,
    neighbours,
    neigh_count,
    energy_ref,
    embed,
    w_lin,
    w_in,
    w_mid,
    w_out,
    w_mix,
    w_site,
):
    kinds = species[0, 0, 0]
    coords = positions[0, 0, 0]
    send_list = send_idx[0, 0, 0]
    neigh = neighbours[0, 0, 0]
    counts = neigh_count[0, 0, 0]
    atoms = kinds.shape[0]
    ghosts = send_list.shape[0]
    table = embed.astype(jnp.float32)
    kind_grid = jnp.arange(table.shape[0], dtype=jnp.float32)
    own_hot = (kinds.astype(jnp.float32)[None, :] == kind_grid[:, None]).astype(jnp.float32)
    base = apply_left(table, own_hot)
    chans = base.shape[0]
    lin_w = w_lin.astype(jnp.float32)
    in_w = w_in.astype(jnp.float32)
    mid_w = w_mid.astype(jnp.float32)
    out_w = w_out.astype(jnp.float32)
    mix_w = w_mix.astype(jnp.float32)
    lifted = rounded(apply_left(lin_w, base))
    send_hot = (send_list[:, None] == lax.broadcasted_iota(jnp.int32, (ghosts, atoms), 1)).astype(
        jnp.float32
    )
    sent_pos = jnp.take(coords, send_list, axis=1)
    shift_rows = jnp.concatenate(
        [
            jnp.broadcast_to(
                jnp.asarray([domain_side * step_x, domain_side * step_y, 0.0], dtype=jnp.float32)[
                    :, None
                ],
                (3, ghosts),
            )
            for step_x, step_y in neighbour_steps
        ],
        axis=1,
    )

    def energy_of(own_feat, own_pos, far_feat, far_pos, p_in, p_mid, p_out, p_mix):
        seen_feat = jnp.concatenate([own_feat, far_feat], axis=1)
        seen_pos = jnp.concatenate([own_pos, far_pos], axis=1)
        return local_energy(
            seen_feat, seen_pos, neigh, counts, base, (p_in, p_mid, p_out, p_mix, w_site)
        )

    payload = jnp.concatenate([jnp.take(lifted, send_list, axis=1), sent_pos], axis=0)[None, None]
    beside_all = with_halo(payload, (("dx", 0), ("dy", 1)), 1)
    received = jnp.concatenate(slot_list(beside_all), axis=1)
    far_feat = received[:chans]
    far_pos = received[chans:] + shift_rows
    local_sum, pullback = jax.vjp(
        energy_of, lifted, coords, far_feat, far_pos, in_w, mid_w, out_w, mix_w
    )
    feat_own, pos_own, feat_far, pos_far, grad_in, grad_mid, grad_out, grad_mix = pullback(
        jnp.ones_like(local_sum)
    )
    slots = fold_slots(jnp.concatenate([feat_far, pos_far], axis=0), ghosts)
    returned = carry_features(slots)
    feat_total = feat_own + jnp.dot(returned[:chans], send_hot, precision=HIGHEST)
    pos_total = pos_own + jnp.dot(returned[chans:], send_hot, precision=HIGHEST)
    kind_sums = lax.dot_general(own_hot, feat_total, (((1,), (1,)), ((), ())), precision=HIGHEST)
    natoms = float(atoms * lax.axis_size("dx") * lax.axis_size("dy"))
    lane = 128
    energy_row = jnp.zeros((1, lane), jnp.float32).at[0, 0].set(local_sum)
    parts = (kind_sums, grad_in, grad_mid, grad_out, grad_mix)
    packed = jnp.concatenate([g.reshape(-1, lane) for g in parts] + [energy_row], axis=0)
    summed = exchange_sum(exchange_sum(packed, "dy"), "dx")
    per_atom = summed[-1, 0] / natoms
    coef = (per_atom - energy_ref[0]) / natoms
    weighted = exchange_sum(coef * summed[:-1], "rep")
    outs = []
    offset = 0
    for g in parts:
        rows = g.size // lane
        outs.append(weighted[offset : offset + rows].reshape(g.shape))
        offset += rows
    grad_lin = lax.dot_general(table, outs[0], (((0,), (0,)), ((), ())), precision=HIGHEST)
    forces = (-pos_total)[None, None, None]
    return (forces, per_atom.reshape(1), grad_lin, outs[1], outs[2], outs[3], outs[4])


def solution(mesh):
    in_specs = (
        P("rep", "dx", "dy", None),
        P("rep", "dx", "dy", None, None),
        P("rep", "dx", "dy", None),
        P("rep", "dx", "dy", None, None),
        P("rep", "dx", "dy", None),
        P("rep"),
        P(),
        P(),
        P(),
        P(),
        P(),
        P(),
        P(),
    )
    out_specs = (P("rep", "dx", "dy", None, None), P("rep"), P(), P(), P(), P(), P())
    return jax.shard_map(body, mesh=mesh, in_specs=in_specs, out_specs=out_specs, check_vma=False)
```

```python
import math

import jax
import jax.numpy as jnp
from jax import lax
from jax.ad_checkpoint import checkpoint_name
from jax.sharding import PartitionSpec as P

HIGHEST = lax.Precision.HIGHEST
cutoff_top = 6.0
cutoff_sq = 36.0
width_gain = 2.0
domain_side = 7.0
root_three = math.sqrt(3.0)
root_five = math.sqrt(5.0)
root_fifteen = math.sqrt(15.0)
saved_names = ("far_pos", "sender", "first", "second", "radial")
neighbour_steps = ((-1, -1), (-1, 0), (-1, 1), (0, -1), (0, 1), (1, -1), (1, 0), (1, 1))


def with_halo(shard, sides, width):
    for axis, dim in sides:
        count, length = (lax.axis_size(axis), shard.shape[dim])
        up = [(i, (i + 1) % count) for i in range(count)]
        down = [(j, i) for i, j in up]
        last = lax.slice_in_dim(shard, length - width, length, axis=dim)
        first = lax.slice_in_dim(shard, 0, width, axis=dim)
        before = lax.ppermute(last, axis, up)
        after = lax.ppermute(first, axis, down)
        shard = jnp.concatenate([before, shard, after], axis=dim)
    return shard


def exchange_sum(values, axis):
    count = lax.axis_size(axis)
    assert count & (count - 1) == 0
    step = 1
    while step < count:
        values = values + lax.ppermute(values, axis, [(i, i ^ step) for i in range(count)])
        step *= 2
    return values


def rounded(values):
    narrow = lax.optimization_barrier(values.astype(jnp.bfloat16))
    return values + lax.stop_gradient(narrow.astype(jnp.float32) - values)


def apply_left(weight, values):
    return lax.dot_general(weight, values, (((0,), (0,)), ((), ())), precision=HIGHEST)


def block_energy(seen_feat, seen_pos, neigh_blk, count_blk, base_blk, own_pos, weights):
    w_in, w_mid, w_out, w_mix, w_site = weights
    slots, atoms_blk = neigh_blk.shape
    chans = base_blk.shape[0]
    flat_index = neigh_blk.reshape(-1)
    far_pos = checkpoint_name(jnp.take(seen_pos, flat_index, axis=1), "far_pos")
    near_pos = jnp.broadcast_to(own_pos[:, None, :], (3, slots, atoms_blk)).reshape(
        3, slots * atoms_blk
    )
    delta = far_pos - near_pos
    dist_sq = jnp.sum(delta * delta, axis=0) + 0.01
    radius = jnp.sqrt(dist_sq)
    unit = delta / radius[None, :]
    nbasis = w_in.shape[0]
    centres = cutoff_top * jnp.arange(nbasis, dtype=jnp.float32) / (nbasis - 1)
    envelope = jnp.maximum(1.0 - dist_sq / cutoff_sq, 0.0) ** 2
    basis = rounded(
        jnp.exp(-width_gain * (radius[None, :] - centres[:, None]) ** 2) * envelope[None, :]
    )
    first = checkpoint_name(rounded(jax.nn.silu(apply_left(w_in, basis))), "first")
    second = checkpoint_name(rounded(jax.nn.silu(apply_left(w_mid, first))), "second")
    radial = checkpoint_name(apply_left(w_out, second), "radial")
    live = (
        (lax.broadcasted_iota(jnp.int32, (slots, atoms_blk), 0) < count_blk[None, :])
        .astype(jnp.float32)
        .reshape(-1)
    )
    sender = checkpoint_name(jnp.take(seen_feat, flat_index, axis=1) * live[None, :], "sender")
    unit_x = unit[0]
    unit_y = unit[1]
    unit_z = unit[2]
    order_one = [root_three * unit_x, root_three * unit_y, root_three * unit_z]
    order_two = [
        root_fifteen * unit_x * unit_y,
        root_fifteen * unit_y * unit_z,
        0.5 * root_five * (3.0 * unit_z * unit_z - 1.0),
        root_fifteen * unit_x * unit_z,
        0.5 * root_fifteen * (unit_x * unit_x - unit_y * unit_y),
    ]
    norm_gain = 1.0 / math.sqrt(slots)

    def pooled(values):
        return jnp.sum(values.reshape(chans, slots, atoms_blk), axis=1) * norm_gain

    scalar_part = pooled(radial[:chans] * sender)
    vector_msg = radial[chans : 2 * chans] * sender
    tensor_msg = radial[2 * chans :] * sender
    vector_part = jnp.zeros_like(scalar_part)
    for harmonic in order_one:
        vector_part = vector_part + pooled(vector_msg * harmonic[None, :]) ** 2
    tensor_part = jnp.zeros_like(scalar_part)
    for harmonic in order_two:
        tensor_part = tensor_part + pooled(tensor_msg * harmonic[None, :]) ** 2
    invariants = rounded(jnp.concatenate([scalar_part, vector_part, tensor_part], axis=0))
    updated = base_blk + apply_left(w_mix, invariants)
    return jnp.sum(w_site[:, None] * jax.nn.silu(updated))


def local_energy(seen_feat, seen_pos, neigh, counts, base, weights):
    atoms = neigh.shape[1]
    block = min(atoms, 128)

    def one_block(index):
        start = index * block
        return block_energy(
            seen_feat,
            seen_pos,
            lax.dynamic_slice_in_dim(neigh, start, block, 1),
            lax.dynamic_slice_in_dim(counts, start, block, 0),
            lax.dynamic_slice_in_dim(base, start, block, 1),
            lax.dynamic_slice_in_dim(seen_pos, start, block, 1),
            weights,
        )

    kept = jax.checkpoint_policies.save_only_these_names(*saved_names)
    return jnp.sum(lax.map(jax.checkpoint(one_block, policy=kept), jnp.arange(atoms // block, dtype=jnp.int32)))


def slot_list(beside_all):
    return [beside_all[step_x + 1, step_y + 1] for step_x, step_y in neighbour_steps]


def fold_slots(blocks, width):
    pieces = [blocks[:, slot * width : (slot + 1) * width] for slot in range(8)]
    empty = jnp.zeros_like(pieces[0])
    ordered = pieces[:4] + [empty] + pieces[4:]
    return jnp.stack(ordered, axis=0).reshape((3, 3) + pieces[0].shape)


def carry_features(slots):
    rows = with_halo(slots, (("dx", 0),), 1)
    merged = slots[1] + rows[0] + rows[4]
    columns = with_halo(merged, (("dy", 0),), 1)
    return merged[1] + columns[0] + columns[4]


def body(
    species,
    positions,
    send_idx,
    neighbours,
    neigh_count,
    energy_ref,
    embed,
    w_lin,
    w_in,
    w_mid,
    w_out,
    w_mix,
    w_site,
):
    kinds = species[0, 0, 0]
    coords = positions[0, 0, 0]
    send_list = send_idx[0, 0, 0]
    neigh = neighbours[0, 0, 0]
    counts = neigh_count[0, 0, 0]
    atoms = kinds.shape[0]
    ghosts = send_list.shape[0]
    table = embed.astype(jnp.float32)
    kind_grid = jnp.arange(table.shape[0], dtype=jnp.float32)
    own_hot = (kinds.astype(jnp.float32)[None, :] == kind_grid[:, None]).astype(jnp.float32)
    base = apply_left(table, own_hot)
    chans = base.shape[0]
    lin_w = w_lin.astype(jnp.float32)
    in_w = w_in.astype(jnp.float32)
    mid_w = w_mid.astype(jnp.float32)
    out_w = w_out.astype(jnp.float32)
    mix_w = w_mix.astype(jnp.float32)
    lifted = rounded(apply_left(lin_w, base))
    send_hot = (send_list[:, None] == lax.broadcasted_iota(jnp.int32, (ghosts, atoms), 1)).astype(
        jnp.float32
    )
    sent_pos = jnp.take(coords, send_list, axis=1)
    shift_rows = jnp.concatenate(
        [
            jnp.broadcast_to(
                jnp.asarray([domain_side * step_x, domain_side * step_y, 0.0], dtype=jnp.float32)[
                    :, None
                ],
                (3, ghosts),
            )
            for step_x, step_y in neighbour_steps
        ],
        axis=1,
    )

    def energy_of(own_feat, own_pos, far_feat, far_pos, p_in, p_mid, p_out, p_mix):
        seen_feat = jnp.concatenate([own_feat, far_feat], axis=1)
        seen_pos = jnp.concatenate([own_pos, far_pos], axis=1)
        return local_energy(
            seen_feat, seen_pos, neigh, counts, base, (p_in, p_mid, p_out, p_mix, w_site)
        )

    payload = jnp.concatenate([jnp.take(lifted, send_list, axis=1), sent_pos], axis=0)[None, None]
    beside_all = with_halo(payload, (("dx", 0), ("dy", 1)), 1)
    received = jnp.concatenate(slot_list(beside_all), axis=1)
    far_feat = received[:chans]
    far_pos = received[chans:] + shift_rows
    local_sum, pullback = jax.vjp(
        energy_of, lifted, coords, far_feat, far_pos, in_w, mid_w, out_w, mix_w
    )
    feat_own, pos_own, feat_far, pos_far, grad_in, grad_mid, grad_out, grad_mix = pullback(
        jnp.ones_like(local_sum)
    )
    slots = fold_slots(jnp.concatenate([feat_far, pos_far], axis=0), ghosts)
    returned = carry_features(slots)
    feat_total = feat_own + jnp.dot(returned[:chans], send_hot, precision=HIGHEST)
    pos_total = pos_own + jnp.dot(returned[chans:], send_hot, precision=HIGHEST)
    kind_sums = lax.dot_general(own_hot, feat_total, (((1,), (1,)), ((), ())), precision=HIGHEST)
    natoms = float(atoms * lax.axis_size("dx") * lax.axis_size("dy"))
    lane = 128
    energy_row = jnp.zeros((1, lane), jnp.float32).at[0, 0].set(local_sum)
    parts = (kind_sums, grad_in, grad_mid, grad_out, grad_mix)
    packed = jnp.concatenate([g.reshape(-1, lane) for g in parts] + [energy_row], axis=0)
    summed = exchange_sum(exchange_sum(packed, "dy"), "dx")
    per_atom = summed[-1, 0] / natoms
    coef = (per_atom - energy_ref[0]) / natoms
    weighted = exchange_sum(coef * summed[:-1], "rep")
    outs = []
    offset = 0
    for g in parts:
        rows = g.size // lane
        outs.append(weighted[offset : offset + rows].reshape(g.shape))
        offset += rows
    grad_lin = lax.dot_general(table, outs[0], (((0,), (0,)), ((), ())), precision=HIGHEST)
    forces = (-pos_total)[None, None, None]
    return (forces, per_atom.reshape(1), grad_lin, outs[1], outs[2], outs[3], outs[4])


def solution(mesh):
    in_specs = (
        P("rep", "dx", "dy", None),
        P("rep", "dx", "dy", None, None),
        P("rep", "dx", "dy", None),
        P("rep", "dx", "dy", None, None),
        P("rep", "dx", "dy", None),
        P("rep"),
        P(),
        P(),
        P(),
        P(),
        P(),
        P(),
        P(),
    )
    out_specs = (P("rep", "dx", "dy", None, None), P("rep"), P(), P(), P(), P(), P())
    return jax.shard_map(body, mesh=mesh, in_specs=in_specs, out_specs=out_specs, check_vma=False)
```

```python
import math

import jax
import jax.numpy as jnp
from jax import lax
from jax.ad_checkpoint import checkpoint_name
from jax.sharding import PartitionSpec as P

HIGHEST = lax.Precision.HIGHEST
cutoff_top = 6.0
cutoff_sq = 36.0
width_gain = 2.0
domain_side = 7.0
root_three = math.sqrt(3.0)
root_five = math.sqrt(5.0)
root_fifteen = math.sqrt(15.0)
saved_names = ("far_pos", "sender", "first", "second", "radial")
neighbour_steps = ((-1, -1), (-1, 0), (-1, 1), (0, -1), (0, 1), (1, -1), (1, 0), (1, 1))


def with_halo(shard, sides, width):
    for axis, dim in sides:
        count, length = (lax.axis_size(axis), shard.shape[dim])
        up = [(i, (i + 1) % count) for i in range(count)]
        down = [(j, i) for i, j in up]
        last = lax.slice_in_dim(shard, length - width, length, axis=dim)
        first = lax.slice_in_dim(shard, 0, width, axis=dim)
        before = lax.ppermute(last, axis, up)
        after = lax.ppermute(first, axis, down)
        shard = jnp.concatenate([before, shard, after], axis=dim)
    return shard


def exchange_sum(values, axis):
    count = lax.axis_size(axis)
    assert count & (count - 1) == 0
    step = 1
    while step < count:
        values = values + lax.ppermute(values, axis, [(i, i ^ step) for i in range(count)])
        step *= 2
    return values


def rounded(values):
    narrow = lax.optimization_barrier(values.astype(jnp.bfloat16))
    return values + lax.stop_gradient(narrow.astype(jnp.float32) - values)


def apply_left(weight, values):
    return lax.dot_general(weight, values, (((0,), (0,)), ((), ())), precision=HIGHEST)


def block_energy(seen_feat, seen_pos, neigh_blk, count_blk, base_blk, own_pos, weights):
    w_in, w_mid, w_out, w_mix, w_site = weights
    slots, atoms_blk = neigh_blk.shape
    chans = base_blk.shape[0]
    flat_index = neigh_blk.reshape(-1)
    far_pos = checkpoint_name(jnp.take(seen_pos, flat_index, axis=1), "far_pos")
    near_pos = jnp.broadcast_to(own_pos[:, None, :], (3, slots, atoms_blk)).reshape(
        3, slots * atoms_blk
    )
    delta = far_pos - near_pos
    dist_sq = jnp.sum(delta * delta, axis=0) + 0.01
    radius = jnp.sqrt(dist_sq)
    unit = delta / radius[None, :]
    nbasis = w_in.shape[0]
    centres = cutoff_top * jnp.arange(nbasis, dtype=jnp.float32) / (nbasis - 1)
    envelope = jnp.maximum(1.0 - dist_sq / cutoff_sq, 0.0) ** 2
    basis = rounded(
        jnp.exp(-width_gain * (radius[None, :] - centres[:, None]) ** 2) * envelope[None, :]
    )
    first = checkpoint_name(rounded(jax.nn.silu(apply_left(w_in, basis))), "first")
    second = checkpoint_name(rounded(jax.nn.silu(apply_left(w_mid, first))), "second")
    radial = checkpoint_name(apply_left(w_out, second), "radial")
    live = (
        (lax.broadcasted_iota(jnp.int32, (slots, atoms_blk), 0) < count_blk[None, :])
        .astype(jnp.float32)
        .reshape(-1)
    )
    sender = checkpoint_name(jnp.take(seen_feat, flat_index, axis=1) * live[None, :], "sender")
    unit_x = unit[0]
    unit_y = unit[1]
    unit_z = unit[2]
    order_one = [root_three * unit_x, root_three * unit_y, root_three * unit_z]
    order_two = [
        root_fifteen * unit_x * unit_y,
        root_fifteen * unit_y * unit_z,
        0.5 * root_five * (3.0 * unit_z * unit_z - 1.0),
        root_fifteen * unit_x * unit_z,
        0.5 * root_fifteen * (unit_x * unit_x - unit_y * unit_y),
    ]
    norm_gain = 1.0 / math.sqrt(slots)

    def pooled(values):
        return jnp.sum(values.reshape(chans, slots, atoms_blk), axis=1) * norm_gain

    scalar_part = pooled(radial[:chans] * sender)
    vector_msg = radial[chans : 2 * chans] * sender
    tensor_msg = radial[2 * chans :] * sender
    vector_part = jnp.zeros_like(scalar_part)
    for harmonic in order_one:
        vector_part = vector_part + pooled(vector_msg * harmonic[None, :]) ** 2
    tensor_part = jnp.zeros_like(scalar_part)
    for harmonic in order_two:
        tensor_part = tensor_part + pooled(tensor_msg * harmonic[None, :]) ** 2
    invariants = rounded(jnp.concatenate([scalar_part, vector_part, tensor_part], axis=0))
    updated = base_blk + apply_left(w_mix, invariants)
    return jnp.sum(w_site[:, None] * jax.nn.silu(updated))


def local_energy(seen_feat, seen_pos, neigh, counts, base, weights):
    atoms = neigh.shape[1]
    block = min(atoms, 256)

    def one_block(index):
        start = index * block
        return block_energy(
            seen_feat,
            seen_pos,
            lax.dynamic_slice_in_dim(neigh, start, block, 1),
            lax.dynamic_slice_in_dim(counts, start, block, 0),
            lax.dynamic_slice_in_dim(base, start, block, 1),
            lax.dynamic_slice_in_dim(seen_pos, start, block, 1),
            weights,
        )

    kept = jax.checkpoint_policies.save_only_these_names(*saved_names)
    return jnp.sum(lax.map(jax.checkpoint(one_block, policy=kept), jnp.arange(atoms // block, dtype=jnp.int32)))


def slot_list(beside_all):
    return [beside_all[step_x + 1, step_y + 1] for step_x, step_y in neighbour_steps]


def fold_slots(blocks, width):
    pieces = [blocks[:, slot * width : (slot + 1) * width] for slot in range(8)]
    empty = jnp.zeros_like(pieces[0])
    ordered = pieces[:4] + [empty] + pieces[4:]
    return jnp.stack(ordered, axis=0).reshape((3, 3) + pieces[0].shape)


def carry_features(slots):
    rows = with_halo(slots, (("dx", 0),), 1)
    merged = slots[1] + rows[0] + rows[4]
    columns = with_halo(merged, (("dy", 0),), 1)
    return merged[1] + columns[0] + columns[4]


def body(
    species,
    positions,
    send_idx,
    neighbours,
    neigh_count,
    energy_ref,
    embed,
    w_lin,
    w_in,
    w_mid,
    w_out,
    w_mix,
    w_site,
):
    kinds = species[0, 0, 0]
    coords = positions[0, 0, 0]
    send_list = send_idx[0, 0, 0]
    neigh = neighbours[0, 0, 0]
    counts = neigh_count[0, 0, 0]
    atoms = kinds.shape[0]
    ghosts = send_list.shape[0]
    table = embed.astype(jnp.float32)
    kind_grid = jnp.arange(table.shape[0], dtype=jnp.float32)
    own_hot = (kinds.astype(jnp.float32)[None, :] == kind_grid[:, None]).astype(jnp.float32)
    base = apply_left(table, own_hot)
    chans = base.shape[0]
    lin_w = w_lin.astype(jnp.float32)
    in_w = w_in.astype(jnp.float32)
    mid_w = w_mid.astype(jnp.float32)
    out_w = w_out.astype(jnp.float32)
    mix_w = w_mix.astype(jnp.float32)
    lifted = rounded(apply_left(lin_w, base))
    send_hot = (send_list[:, None] == lax.broadcasted_iota(jnp.int32, (ghosts, atoms), 1)).astype(
        jnp.float32
    )
    sent_pos = jnp.take(coords, send_list, axis=1)
    shift_rows = jnp.concatenate(
        [
            jnp.broadcast_to(
                jnp.asarray([domain_side * step_x, domain_side * step_y, 0.0], dtype=jnp.float32)[
                    :, None
                ],
                (3, ghosts),
            )
            for step_x, step_y in neighbour_steps
        ],
        axis=1,
    )

    def energy_of(own_feat, own_pos, far_feat, far_pos, p_in, p_mid, p_out, p_mix):
        seen_feat = jnp.concatenate([own_feat, far_feat], axis=1)
        seen_pos = jnp.concatenate([own_pos, far_pos], axis=1)
        return local_energy(
            seen_feat, seen_pos, neigh, counts, base, (p_in, p_mid, p_out, p_mix, w_site)
        )

    payload = jnp.concatenate([jnp.take(lifted, send_list, axis=1), sent_pos], axis=0)[None, None]
    beside_all = with_halo(payload, (("dx", 0), ("dy", 1)), 1)
    received = jnp.concatenate(slot_list(beside_all), axis=1)
    far_feat = received[:chans]
    far_pos = received[chans:] + shift_rows
    local_sum, pullback = jax.vjp(
        energy_of, lifted, coords, far_feat, far_pos, in_w, mid_w, out_w, mix_w
    )
    feat_own, pos_own, feat_far, pos_far, grad_in, grad_mid, grad_out, grad_mix = pullback(
        jnp.ones_like(local_sum)
    )
    slots = fold_slots(jnp.concatenate([feat_far, pos_far], axis=0), ghosts)
    returned = carry_features(slots)
    feat_total = feat_own + jnp.dot(returned[:chans], send_hot, precision=HIGHEST)
    pos_total = pos_own + jnp.dot(returned[chans:], send_hot, precision=HIGHEST)
    kind_sums = lax.dot_general(own_hot, feat_total, (((1,), (1,)), ((), ())), precision=HIGHEST)
    natoms = float(atoms * lax.axis_size("dx") * lax.axis_size("dy"))
    lane = 128
    energy_row = jnp.zeros((1, lane), jnp.float32).at[0, 0].set(local_sum)
    parts = (kind_sums, grad_in, grad_mid, grad_out, grad_mix)
    packed = jnp.concatenate([g.reshape(-1, lane) for g in parts] + [energy_row], axis=0)
    summed = exchange_sum(exchange_sum(packed, "dy"), "dx")
    per_atom = summed[-1, 0] / natoms
    coef = (per_atom - energy_ref[0]) / natoms
    weighted = exchange_sum(coef * summed[:-1], "rep")
    outs = []
    offset = 0
    for g in parts:
        rows = g.size // lane
        outs.append(weighted[offset : offset + rows].reshape(g.shape))
        offset += rows
    grad_lin = lax.dot_general(table, outs[0], (((0,), (0,)), ((), ())), precision=HIGHEST)
    forces = (-pos_total)[None, None, None]
    return (forces, per_atom.reshape(1), grad_lin, outs[1], outs[2], outs[3], outs[4])


def solution(mesh):
    in_specs = (
        P("rep", "dx", "dy", None),
        P("rep", "dx", "dy", None, None),
        P("rep", "dx", "dy", None),
        P("rep", "dx", "dy", None, None),
        P("rep", "dx", "dy", None),
        P("rep"),
        P(),
        P(),
        P(),
        P(),
        P(),
        P(),
        P(),
    )
    out_specs = (P("rep", "dx", "dy", None, None), P("rep"), P(), P(), P(), P(), P())
    return jax.shard_map(body, mesh=mesh, in_specs=in_specs, out_specs=out_specs, check_vma=False)
```

```python
import math

import jax
import jax.numpy as jnp
from jax import lax
from jax.ad_checkpoint import checkpoint_name
from jax.sharding import PartitionSpec as P

HIGHEST = lax.Precision.HIGHEST
cutoff_top = 6.0
cutoff_sq = 36.0
width_gain = 2.0
domain_side = 7.0
root_three = math.sqrt(3.0)
root_five = math.sqrt(5.0)
root_fifteen = math.sqrt(15.0)
saved_names = ("far_pos", "sender", "first", "second", "radial")
neighbour_steps = ((-1, -1), (-1, 0), (-1, 1), (0, -1), (0, 1), (1, -1), (1, 0), (1, 1))


def with_halo(shard, sides, width):
    for axis, dim in sides:
        count, length = (lax.axis_size(axis), shard.shape[dim])
        up = [(i, (i + 1) % count) for i in range(count)]
        down = [(j, i) for i, j in up]
        last = lax.slice_in_dim(shard, length - width, length, axis=dim)
        first = lax.slice_in_dim(shard, 0, width, axis=dim)
        before = lax.ppermute(last, axis, up)
        after = lax.ppermute(first, axis, down)
        shard = jnp.concatenate([before, shard, after], axis=dim)
    return shard


def exchange_sum(values, axis):
    count = lax.axis_size(axis)
    assert count & (count - 1) == 0
    step = 1
    while step < count:
        values = values + lax.ppermute(values, axis, [(i, i ^ step) for i in range(count)])
        step *= 2
    return values


def rounded(values):
    narrow = lax.optimization_barrier(values.astype(jnp.bfloat16))
    return values + lax.stop_gradient(narrow.astype(jnp.float32) - values)


def apply_left(weight, values):
    return lax.dot_general(weight, values, (((0,), (0,)), ((), ())), precision=HIGHEST)


def block_energy(seen_feat, seen_pos, neigh_blk, count_blk, base_blk, own_pos, weights):
    w_in, w_mid, w_out, w_mix, w_site = weights
    slots, atoms_blk = neigh_blk.shape
    chans = base_blk.shape[0]
    flat_index = neigh_blk.reshape(-1)
    far_pos = checkpoint_name(jnp.take(seen_pos, flat_index, axis=1), "far_pos")
    near_pos = jnp.broadcast_to(own_pos[:, None, :], (3, slots, atoms_blk)).reshape(
        3, slots * atoms_blk
    )
    delta = far_pos - near_pos
    dist_sq = jnp.sum(delta * delta, axis=0) + 0.01
    radius = jnp.sqrt(dist_sq)
    unit = delta / radius[None, :]
    nbasis = w_in.shape[0]
    centres = cutoff_top * jnp.arange(nbasis, dtype=jnp.float32) / (nbasis - 1)
    envelope = jnp.maximum(1.0 - dist_sq / cutoff_sq, 0.0) ** 2
    basis = rounded(
        jnp.exp(-width_gain * (radius[None, :] - centres[:, None]) ** 2) * envelope[None, :]
    )
    first = checkpoint_name(rounded(jax.nn.silu(apply_left(w_in, basis))), "first")
    second = checkpoint_name(rounded(jax.nn.silu(apply_left(w_mid, first))), "second")
    radial = checkpoint_name(apply_left(w_out, second), "radial")
    live = (
        (lax.broadcasted_iota(jnp.int32, (slots, atoms_blk), 0) < count_blk[None, :])
        .astype(jnp.float32)
        .reshape(-1)
    )
    sender = checkpoint_name(jnp.take(seen_feat, flat_index, axis=1) * live[None, :], "sender")
    unit_x = unit[0]
    unit_y = unit[1]
    unit_z = unit[2]
    order_one = [root_three * unit_x, root_three * unit_y, root_three * unit_z]
    order_two = [
        root_fifteen * unit_x * unit_y,
        root_fifteen * unit_y * unit_z,
        0.5 * root_five * (3.0 * unit_z * unit_z - 1.0),
        root_fifteen * unit_x * unit_z,
        0.5 * root_fifteen * (unit_x * unit_x - unit_y * unit_y),
    ]
    norm_gain = 1.0 / math.sqrt(slots)

    def pooled(values):
        return jnp.sum(values.reshape(chans, slots, atoms_blk), axis=1) * norm_gain

    scalar_part = pooled(radial[:chans] * sender)
    vector_msg = radial[chans : 2 * chans] * sender
    tensor_msg = radial[2 * chans :] * sender
    vector_part = jnp.zeros_like(scalar_part)
    for harmonic in order_one:
        vector_part = vector_part + pooled(vector_msg * harmonic[None, :]) ** 2
    tensor_part = jnp.zeros_like(scalar_part)
    for harmonic in order_two:
        tensor_part = tensor_part + pooled(tensor_msg * harmonic[None, :]) ** 2
    invariants = rounded(jnp.concatenate([scalar_part, vector_part, tensor_part], axis=0))
    updated = base_blk + apply_left(w_mix, invariants)
    return jnp.sum(w_site[:, None] * jax.nn.silu(updated))


def local_energy(seen_feat, seen_pos, neigh, counts, base, weights):
    atoms = neigh.shape[1]
    block = min(atoms, 256)

    def one_block(index):
        start = index * block
        return block_energy(
            seen_feat,
            seen_pos,
            lax.dynamic_slice_in_dim(neigh, start, block, 1),
            lax.dynamic_slice_in_dim(counts, start, block, 0),
            lax.dynamic_slice_in_dim(base, start, block, 1),
            lax.dynamic_slice_in_dim(seen_pos, start, block, 1),
            weights,
        )

    kept = jax.checkpoint_policies.save_only_these_names(*saved_names)
    return jnp.sum(lax.map(one_block, jnp.arange(atoms // block, dtype=jnp.int32)))


def slot_list(beside_all):
    return [beside_all[step_x + 1, step_y + 1] for step_x, step_y in neighbour_steps]


def fold_slots(blocks, width):
    pieces = [blocks[:, slot * width : (slot + 1) * width] for slot in range(8)]
    empty = jnp.zeros_like(pieces[0])
    ordered = pieces[:4] + [empty] + pieces[4:]
    return jnp.stack(ordered, axis=0).reshape((3, 3) + pieces[0].shape)


def carry_features(slots):
    rows = with_halo(slots, (("dx", 0),), 1)
    merged = slots[1] + rows[0] + rows[4]
    columns = with_halo(merged, (("dy", 0),), 1)
    return merged[1] + columns[0] + columns[4]


def body(
    species,
    positions,
    send_idx,
    neighbours,
    neigh_count,
    energy_ref,
    embed,
    w_lin,
    w_in,
    w_mid,
    w_out,
    w_mix,
    w_site,
):
    kinds = species[0, 0, 0]
    coords = positions[0, 0, 0]
    send_list = send_idx[0, 0, 0]
    neigh = neighbours[0, 0, 0]
    counts = neigh_count[0, 0, 0]
    atoms = kinds.shape[0]
    ghosts = send_list.shape[0]
    table = embed.astype(jnp.float32)
    kind_grid = jnp.arange(table.shape[0], dtype=jnp.float32)
    own_hot = (kinds.astype(jnp.float32)[None, :] == kind_grid[:, None]).astype(jnp.float32)
    base = apply_left(table, own_hot)
    chans = base.shape[0]
    lin_w = w_lin.astype(jnp.float32)
    in_w = w_in.astype(jnp.float32)
    mid_w = w_mid.astype(jnp.float32)
    out_w = w_out.astype(jnp.float32)
    mix_w = w_mix.astype(jnp.float32)
    lifted = rounded(apply_left(lin_w, base))
    send_hot = (send_list[:, None] == lax.broadcasted_iota(jnp.int32, (ghosts, atoms), 1)).astype(
        jnp.float32
    )
    sent_pos = jnp.take(coords, send_list, axis=1)
    shift_rows = jnp.concatenate(
        [
            jnp.broadcast_to(
                jnp.asarray([domain_side * step_x, domain_side * step_y, 0.0], dtype=jnp.float32)[
                    :, None
                ],
                (3, ghosts),
            )
            for step_x, step_y in neighbour_steps
        ],
        axis=1,
    )

    def energy_of(own_feat, own_pos, far_feat, far_pos, p_in, p_mid, p_out, p_mix):
        seen_feat = jnp.concatenate([own_feat, far_feat], axis=1)
        seen_pos = jnp.concatenate([own_pos, far_pos], axis=1)
        return local_energy(
            seen_feat, seen_pos, neigh, counts, base, (p_in, p_mid, p_out, p_mix, w_site)
        )

    payload = jnp.concatenate([jnp.take(lifted, send_list, axis=1), sent_pos], axis=0)[None, None]
    beside_all = with_halo(payload, (("dx", 0), ("dy", 1)), 1)
    received = jnp.concatenate(slot_list(beside_all), axis=1)
    far_feat = received[:chans]
    far_pos = received[chans:] + shift_rows
    local_sum, pullback = jax.vjp(
        energy_of, lifted, coords, far_feat, far_pos, in_w, mid_w, out_w, mix_w
    )
    feat_own, pos_own, feat_far, pos_far, grad_in, grad_mid, grad_out, grad_mix = pullback(
        jnp.ones_like(local_sum)
    )
    slots = fold_slots(jnp.concatenate([feat_far, pos_far], axis=0), ghosts)
    returned = carry_features(slots)
    feat_total = feat_own + jnp.dot(returned[:chans], send_hot, precision=HIGHEST)
    pos_total = pos_own + jnp.dot(returned[chans:], send_hot, precision=HIGHEST)
    kind_sums = lax.dot_general(own_hot, feat_total, (((1,), (1,)), ((), ())), precision=HIGHEST)
    natoms = float(atoms * lax.axis_size("dx") * lax.axis_size("dy"))
    lane = 128
    energy_row = jnp.zeros((1, lane), jnp.float32).at[0, 0].set(local_sum)
    parts = (kind_sums, grad_in, grad_mid, grad_out, grad_mix)
    packed = jnp.concatenate([g.reshape(-1, lane) for g in parts] + [energy_row], axis=0)
    summed = exchange_sum(exchange_sum(packed, "dy"), "dx")
    per_atom = summed[-1, 0] / natoms
    coef = (per_atom - energy_ref[0]) / natoms
    weighted = exchange_sum(coef * summed[:-1], "rep")
    outs = []
    offset = 0
    for g in parts:
        rows = g.size // lane
        outs.append(weighted[offset : offset + rows].reshape(g.shape))
        offset += rows
    grad_lin = lax.dot_general(table, outs[0], (((0,), (0,)), ((), ())), precision=HIGHEST)
    forces = (-pos_total)[None, None, None]
    return (forces, per_atom.reshape(1), grad_lin, outs[1], outs[2], outs[3], outs[4])


def solution(mesh):
    in_specs = (
        P("rep", "dx", "dy", None),
        P("rep", "dx", "dy", None, None),
        P("rep", "dx", "dy", None),
        P("rep", "dx", "dy", None, None),
        P("rep", "dx", "dy", None),
        P("rep"),
        P(),
        P(),
        P(),
        P(),
        P(),
        P(),
        P(),
    )
    out_specs = (P("rep", "dx", "dy", None, None), P("rep"), P(), P(), P(), P(), P())
    return jax.shard_map(body, mesh=mesh, in_specs=in_specs, out_specs=out_specs, check_vma=False)
```

```python
import math

import jax
import jax.numpy as jnp
from jax import lax
from jax.ad_checkpoint import checkpoint_name
from jax.sharding import PartitionSpec as P

HIGHEST = lax.Precision.HIGHEST
cutoff_top = 6.0
cutoff_sq = 36.0
width_gain = 2.0
domain_side = 7.0
root_three = math.sqrt(3.0)
root_five = math.sqrt(5.0)
root_fifteen = math.sqrt(15.0)
saved_names = ("far_pos", "sender", "first", "second", "radial")
neighbour_steps = ((-1, -1), (-1, 0), (-1, 1), (0, -1), (0, 1), (1, -1), (1, 0), (1, 1))


def with_halo(shard, sides, width):
    for axis, dim in sides:
        count, length = (lax.axis_size(axis), shard.shape[dim])
        up = [(i, (i + 1) % count) for i in range(count)]
        down = [(j, i) for i, j in up]
        last = lax.slice_in_dim(shard, length - width, length, axis=dim)
        first = lax.slice_in_dim(shard, 0, width, axis=dim)
        before = lax.ppermute(last, axis, up)
        after = lax.ppermute(first, axis, down)
        shard = jnp.concatenate([before, shard, after], axis=dim)
    return shard


def exchange_sum(values, axis):
    count = lax.axis_size(axis)
    assert count & (count - 1) == 0
    step = 1
    while step < count:
        values = values + lax.ppermute(values, axis, [(i, i ^ step) for i in range(count)])
        step *= 2
    return values


def rounded(values):
    narrow = lax.optimization_barrier(values.astype(jnp.bfloat16))
    return values + lax.stop_gradient(narrow.astype(jnp.float32) - values)


def apply_left(weight, values):
    return lax.dot_general(weight, values, (((0,), (0,)), ((), ())), precision=HIGHEST)


def block_energy(seen_feat, seen_pos, neigh_blk, count_blk, base_blk, own_pos, weights):
    w_in, w_mid, w_out, w_mix, w_site = weights
    slots, atoms_blk = neigh_blk.shape
    chans = base_blk.shape[0]
    flat_index = neigh_blk.reshape(-1)
    seen_hot = (
        lax.broadcasted_iota(jnp.int32, (seen_pos.shape[1], flat_index.shape[0]), 0) == flat_index[None, :]
    ).astype(jnp.float32)
    far_pos = checkpoint_name(jnp.dot(seen_pos, seen_hot, precision=HIGHEST), "far_pos")
    near_pos = jnp.broadcast_to(own_pos[:, None, :], (3, slots, atoms_blk)).reshape(
        3, slots * atoms_blk
    )
    delta = far_pos - near_pos
    dist_sq = jnp.sum(delta * delta, axis=0) + 0.01
    radius = jnp.sqrt(dist_sq)
    unit = delta / radius[None, :]
    nbasis = w_in.shape[0]
    centres = cutoff_top * jnp.arange(nbasis, dtype=jnp.float32) / (nbasis - 1)
    envelope = jnp.maximum(1.0 - dist_sq / cutoff_sq, 0.0) ** 2
    basis = rounded(
        jnp.exp(-width_gain * (radius[None, :] - centres[:, None]) ** 2) * envelope[None, :]
    )
    first = checkpoint_name(rounded(jax.nn.silu(apply_left(w_in, basis))), "first")
    second = checkpoint_name(rounded(jax.nn.silu(apply_left(w_mid, first))), "second")
    radial = checkpoint_name(apply_left(w_out, second), "radial")
    live = (
        (lax.broadcasted_iota(jnp.int32, (slots, atoms_blk), 0) < count_blk[None, :])
        .astype(jnp.float32)
        .reshape(-1)
    )
    sender = checkpoint_name(jnp.take(seen_feat, flat_index, axis=1) * live[None, :], "sender")
    unit_x = unit[0]
    unit_y = unit[1]
    unit_z = unit[2]
    order_one = [root_three * unit_x, root_three * unit_y, root_three * unit_z]
    order_two = [
        root_fifteen * unit_x * unit_y,
        root_fifteen * unit_y * unit_z,
        0.5 * root_five * (3.0 * unit_z * unit_z - 1.0),
        root_fifteen * unit_x * unit_z,
        0.5 * root_fifteen * (unit_x * unit_x - unit_y * unit_y),
    ]
    norm_gain = 1.0 / math.sqrt(slots)

    def pooled(values):
        return jnp.sum(values.reshape(chans, slots, atoms_blk), axis=1) * norm_gain

    scalar_part = pooled(radial[:chans] * sender)
    vector_msg = radial[chans : 2 * chans] * sender
    tensor_msg = radial[2 * chans :] * sender
    vector_part = jnp.zeros_like(scalar_part)
    for harmonic in order_one:
        vector_part = vector_part + pooled(vector_msg * harmonic[None, :]) ** 2
    tensor_part = jnp.zeros_like(scalar_part)
    for harmonic in order_two:
        tensor_part = tensor_part + pooled(tensor_msg * harmonic[None, :]) ** 2
    invariants = rounded(jnp.concatenate([scalar_part, vector_part, tensor_part], axis=0))
    updated = base_blk + apply_left(w_mix, invariants)
    return jnp.sum(w_site[:, None] * jax.nn.silu(updated))


def local_energy(seen_feat, seen_pos, neigh, counts, base, weights):
    atoms = neigh.shape[1]
    block = min(atoms, 256)

    def one_block(index):
        start = index * block
        return block_energy(
            seen_feat,
            seen_pos,
            lax.dynamic_slice_in_dim(neigh, start, block, 1),
            lax.dynamic_slice_in_dim(counts, start, block, 0),
            lax.dynamic_slice_in_dim(base, start, block, 1),
            lax.dynamic_slice_in_dim(seen_pos, start, block, 1),
            weights,
        )

    kept = jax.checkpoint_policies.save_only_these_names(*saved_names)
    return jnp.sum(lax.map(one_block, jnp.arange(atoms // block, dtype=jnp.int32)))


def slot_list(beside_all):
    return [beside_all[step_x + 1, step_y + 1] for step_x, step_y in neighbour_steps]


def fold_slots(blocks, width):
    pieces = [blocks[:, slot * width : (slot + 1) * width] for slot in range(8)]
    empty = jnp.zeros_like(pieces[0])
    ordered = pieces[:4] + [empty] + pieces[4:]
    return jnp.stack(ordered, axis=0).reshape((3, 3) + pieces[0].shape)


def carry_features(slots):
    rows = with_halo(slots, (("dx", 0),), 1)
    merged = slots[1] + rows[0] + rows[4]
    columns = with_halo(merged, (("dy", 0),), 1)
    return merged[1] + columns[0] + columns[4]


def body(
    species,
    positions,
    send_idx,
    neighbours,
    neigh_count,
    energy_ref,
    embed,
    w_lin,
    w_in,
    w_mid,
    w_out,
    w_mix,
    w_site,
):
    kinds = species[0, 0, 0]
    coords = positions[0, 0, 0]
    send_list = send_idx[0, 0, 0]
    neigh = neighbours[0, 0, 0]
    counts = neigh_count[0, 0, 0]
    atoms = kinds.shape[0]
    ghosts = send_list.shape[0]
    table = embed.astype(jnp.float32)
    kind_grid = jnp.arange(table.shape[0], dtype=jnp.float32)
    own_hot = (kinds.astype(jnp.float32)[None, :] == kind_grid[:, None]).astype(jnp.float32)
    base = apply_left(table, own_hot)
    chans = base.shape[0]
    lin_w = w_lin.astype(jnp.float32)
    in_w = w_in.astype(jnp.float32)
    mid_w = w_mid.astype(jnp.float32)
    out_w = w_out.astype(jnp.float32)
    mix_w = w_mix.astype(jnp.float32)
    lifted = rounded(apply_left(lin_w, base))
    send_hot = (send_list[:, None] == lax.broadcasted_iota(jnp.int32, (ghosts, atoms), 1)).astype(
        jnp.float32
    )
    sent_pos = jnp.take(coords, send_list, axis=1)
    shift_rows = jnp.concatenate(
        [
            jnp.broadcast_to(
                jnp.asarray([domain_side * step_x, domain_side * step_y, 0.0], dtype=jnp.float32)[
                    :, None
                ],
                (3, ghosts),
            )
            for step_x, step_y in neighbour_steps
        ],
        axis=1,
    )

    def energy_of(own_feat, own_pos, far_feat, far_pos, p_in, p_mid, p_out, p_mix):
        seen_feat = jnp.concatenate([own_feat, far_feat], axis=1)
        seen_pos = jnp.concatenate([own_pos, far_pos], axis=1)
        return local_energy(
            seen_feat, seen_pos, neigh, counts, base, (p_in, p_mid, p_out, p_mix, w_site)
        )

    payload = jnp.concatenate([jnp.take(lifted, send_list, axis=1), sent_pos], axis=0)[None, None]
    beside_all = with_halo(payload, (("dx", 0), ("dy", 1)), 1)
    received = jnp.concatenate(slot_list(beside_all), axis=1)
    far_feat = received[:chans]
    far_pos = received[chans:] + shift_rows
    local_sum, pullback = jax.vjp(
        energy_of, lifted, coords, far_feat, far_pos, in_w, mid_w, out_w, mix_w
    )
    feat_own, pos_own, feat_far, pos_far, grad_in, grad_mid, grad_out, grad_mix = pullback(
        jnp.ones_like(local_sum)
    )
    slots = fold_slots(jnp.concatenate([feat_far, pos_far], axis=0), ghosts)
    returned = carry_features(slots)
    feat_total = feat_own + jnp.dot(returned[:chans], send_hot, precision=HIGHEST)
    pos_total = pos_own + jnp.dot(returned[chans:], send_hot, precision=HIGHEST)
    kind_sums = lax.dot_general(own_hot, feat_total, (((1,), (1,)), ((), ())), precision=HIGHEST)
    natoms = float(atoms * lax.axis_size("dx") * lax.axis_size("dy"))
    lane = 128
    energy_row = jnp.zeros((1, lane), jnp.float32).at[0, 0].set(local_sum)
    parts = (kind_sums, grad_in, grad_mid, grad_out, grad_mix)
    packed = jnp.concatenate([g.reshape(-1, lane) for g in parts] + [energy_row], axis=0)
    summed = exchange_sum(exchange_sum(packed, "dy"), "dx")
    per_atom = summed[-1, 0] / natoms
    coef = (per_atom - energy_ref[0]) / natoms
    weighted = exchange_sum(coef * summed[:-1], "rep")
    outs = []
    offset = 0
    for g in parts:
        rows = g.size // lane
        outs.append(weighted[offset : offset + rows].reshape(g.shape))
        offset += rows
    grad_lin = lax.dot_general(table, outs[0], (((0,), (0,)), ((), ())), precision=HIGHEST)
    forces = (-pos_total)[None, None, None]
    return (forces, per_atom.reshape(1), grad_lin, outs[1], outs[2], outs[3], outs[4])


def solution(mesh):
    in_specs = (
        P("rep", "dx", "dy", None),
        P("rep", "dx", "dy", None, None),
        P("rep", "dx", "dy", None),
        P("rep", "dx", "dy", None, None),
        P("rep", "dx", "dy", None),
        P("rep"),
        P(),
        P(),
        P(),
        P(),
        P(),
        P(),
        P(),
    )
    out_specs = (P("rep", "dx", "dy", None, None), P("rep"), P(), P(), P(), P(), P())
    return jax.shard_map(body, mesh=mesh, in_specs=in_specs, out_specs=out_specs, check_vma=False)
```
